256 devices in a mesh: section: 8 (over x, core), expert: 32 (over z, y).
Axes of the slice: x: 4, y: 4, z: 8, core: 2. Of those that a mesh axis runs over, the one named last changes fastest.
Arguments:
- tokens: bfloat16 [8, 2304, 2048], P(None, 'expert'), may hold values from -6 to 6
- w_in: bfloat16 [8, 2048, 2048], P('section', 'expert'), may hold values from -0.125 to 0.125
- w_out: bfloat16 [8, 2048, 2048], P('section', 'expert'), may hold values from -0.125 to 0.125
- router: bfloat16 [2048, 32], replicated, may hold values from -0.125 to 0.125
- exp_in: bfloat16 [32, 2048, 2048], P('expert', None, 'section'), may hold values from -0.125 to 0.125
- exp_out: bfloat16 [32, 2048, 2048], P('expert', 'section'), may hold values from -0.375 to 0.375
- active_rows: int32 [4608], P('expert'), may hold values from 0 to 575, as said below
- active_expert: int32 [4608, 1], P('expert'), may hold values from 0 to 31; in each aligned block of 144 rows (0 to 143, 144 to 287, ...) at most 13 rows name the same one
Outputs:
- updated: bfloat16 [8, 2304, 2048], P(None, 'expert', 'section')
The draws below stay inside these ranges and needn't reach their ends.
Inputs may be any that keep to these rules, and one draw needn't show every extreme that they name: `active_rows`: the 144 entries of one token block name distinct rows of its 576 rows. `active_expert`: among the 144 entries of one token block no expert is named more than 13 times.
All inputs are finite; a program needn't handle non-finite values.
Results may differ from the reference program's by a relative error of at most 0.024.
Values may be sent and summed in bfloat16 or wider, within the bound.
No kernel may reach another device: no remote copies, remote signals or barrier semaphores. Data moves between devices by JAX's collectives and lax.ppermute only.
A program may use at most 64 MiB of HBM per device.

```python
import math
import jax
import jax.numpy as jnp
import numpy as np
from jax import lax

D = 2048
HID = 2048
EXP_HID = 2048
MB = 8
TOK_DEV = 72
LAYERS = 8
EXPERTS = 32
TOKENS = 2304
ROWS_DEV = 576
ACT_DEV = 144
ACTIVE = 4608
CAP = 13
N_EXPERT = 32


def force_member(listing, value):
    present = jnp.any(listing == value)
    return jnp.where(present, listing, listing.at[0].set(value))


def draw_active_rows(key, part):
    keys = jax.random.split(jax.random.fold_in(key, 11), N_EXPERT)

    def one_block(block_key):
        return jax.random.permutation(block_key, ROWS_DEV)[:ACT_DEV].astype(jnp.int32)
    lists = jax.vmap(one_block)(keys)
    lists = lists.at[0].set(force_member(lists[0], ROWS_DEV - 1))
    lists = lists.at[N_EXPERT - 1].set(force_member(lists[N_EXPERT - 1], 0))
    return lists.reshape(ACTIVE).astype(jnp.int32)


def raised(drawn, own_key, source, target, blocks, factor):
    def block_of(dim):
        return (jnp.arange(drawn.shape[dim]) // (drawn.shape[dim] // blocks)).reshape((-1,) + (1,) * (drawn.ndim - 1 - dim))

    first = jax.random.permutation(own_key, blocks)[block_of(target)]
    far = (block_of(target) + blocks // 2) % blocks
    return jnp.where((block_of(source) == first) | (block_of(source) == far), factor * drawn, drawn)


def steps_of(key, shape, pieces, least, top_value):
    level = 1.0
    for dim, blocks in pieces:
        draws = jax.random.uniform(jax.random.fold_in(jax.random.fold_in(key, 6), dim), (blocks,), jnp.float32, least / len(pieces), top_value / len(pieces))
        level = level * jnp.repeat(jnp.exp(draws), shape[dim] // blocks).reshape((-1,) + (1,) * (len(shape) - 1 - dim))
    return level


def shared_out(rng, own, number, rows, count, top, limit, skew):
    sequence = jax.random.permutation(rng, count)
    heavy_load, ordinary = load_shares(count, rows * top, limit, skew, True), load_shares(count, rows * top, limit, skew, False)
    places = jnp.arange(count)

    def named(tallies, offset_by):
        used = int((tallies > 0).sum())
        fixed = max(1, used // 4)
        shifted = fixed + (places - fixed + offset_by * (used - fixed)) % max(1, count - fixed)
        return jnp.zeros((count,), jnp.int32).at[sequence[jnp.where(places < fixed, places, shifted)]].set(jnp.asarray(tallies, jnp.int32))

    tallies = jnp.where(number % 4 == 0, named(heavy_load, number // 4), named(ordinary, number - number // 4 - 1))
    mixed = jax.random.permutation(jax.random.fold_in(own, 3), count)
    source_of, receiver = mixed[0:count // 2 * 2:2], mixed[1:count // 2 * 2:2]
    room = jnp.minimum(tallies[source_of] - 1, limit - tallies[receiver]) // 2
    room = jnp.where((source_of == sequence[0]) | (receiver == sequence[0]) | (tallies[receiver] == 0), 0, jnp.maximum(room, 0))
    shifted = jax.random.randint(jax.random.fold_in(own, 4), (count // 2,), 0, 1 << 20) % (room + 1)
    tallies = tallies.at[source_of].add(-shifted).at[receiver].add(shifted)
    items = jnp.searchsorted(jnp.cumsum(tallies), jnp.arange(rows * top), side="right").astype(jnp.int32)
    grid = items.reshape(top, rows).T
    grid = grid[jax.random.permutation(jax.random.fold_in(own, 1), rows)]
    offset_by = jax.random.randint(jax.random.fold_in(own, 2), (rows, 1), 0, top)
    return jnp.take_along_axis(grid, (jnp.arange(top)[None, :] + offset_by) % top, axis=1)


def load_shares(amount, total, most, lean, full):
    loads = [(1 << 20) // math.isqrt(rank ** lean) + 1 for rank in range(1, amount + 1)]
    largest = most if full else min(most, max(-(-total // amount), total * loads[0] // sum(loads)))
    least = 1 if total - largest >= amount - 1 else 0
    holding, surplus = [largest] + [least] * (amount - 1), total - largest - least * (amount - 1)
    while surplus > 0:
        candidates = [i for i in range(1, amount) if holding[i] < largest] or [i for i in range(1, amount) if holding[i] < most]
        mass, left = sum([loads[i] for i in candidates]), surplus
        for i in candidates:
            extra = min(most - holding[i], max(1, left * loads[i] // mass), surplus)
            holding[i] = holding[i] + extra
            surplus = surplus - extra
    return np.array(holding)


def normal_values(rng, dims, scale, reach, cuts=(), held_as=jnp.bfloat16):
    loudness = steps_of(rng, dims, cuts, -0.22, 0.18) if cuts else 1.0
    result = jax.random.normal(rng, dims, jnp.float32) * scale * loudness
    return jnp.minimum(jnp.maximum(result, -reach), reach).astype(held_as)


def heavy_noise(rng, dims, scale, bound, cuts, heavy, kind=jnp.bfloat16):
    values = scale * jax.random.normal(rng, dims, jnp.float32)
    if cuts:
        values = values * steps_of(rng, dims, cuts, -0.22, 0.18)
    return jnp.clip(raised(values, jax.random.fold_in(rng, 3), *heavy), -bound, bound).astype(kind)


def setup_inputs(seed: int = 0) -> dict:
    key_list = jax.random.split(jax.random.key(seed), 9)
    tokens = normal_values(key_list[0], (MB, TOKENS, D), 1.0, 6.0, ((1, 32),))
    w_in = normal_values(key_list[1], (LAYERS, D, HID), D ** -0.5, 0.125, ((0, 8), (1, 32)))
    w_out = normal_values(key_list[2], (LAYERS, HID, D), HID ** -0.5, 0.125, ((0, 8), (1, 32)))
    router = normal_values(key_list[3], (D, EXPERTS), D ** -0.5, 0.125)
    exp_in = normal_values(key_list[4], (EXPERTS, D, EXP_HID), D ** -0.5, 0.125, ((0, 32), (2, 8)))
    exp_out = heavy_noise(key_list[5], (EXPERTS, EXP_HID, D), (EXP_HID // 4) ** -0.5, 0.375, ((0, 32), (1, 8)), (1, 2, 8, 2.0))
    active_rows = draw_active_rows(jax.random.fold_in(key_list[8], 71), 0)
    active_expert_keys = jax.random.split(jax.random.fold_in(key_list[7], 1), ACTIVE // ACT_DEV)
    active_expert_turns = jax.random.permutation(jax.random.fold_in(key_list[7], 3), ACTIVE // ACT_DEV)
    active_expert = jax.vmap(lambda own, number: shared_out(jax.random.fold_in(key_list[7], 2), own, number, ACT_DEV, EXPERTS, 1, CAP, 2))(active_expert_keys, active_expert_turns).reshape((ACTIVE, 1))
    return {"tokens": tokens, "w_in": w_in, "w_out": w_out, "router": router, "exp_in": exp_in, "exp_out": exp_out, "active_rows": active_rows, "active_expert": active_expert}


def normalize(rows):
    wide = rows.astype(jnp.float32)
    scale = lax.rsqrt(lax.optimization_barrier(jnp.mean(wide * wide, axis=-1, keepdims=True)) + 1e-05)
    return wide * scale

def processor(stream, w_first, w_second):
    normed = normalize(stream).astype(jnp.bfloat16)
    hidden = jax.nn.silu(jnp.dot(normed, w_first, preferred_element_type=jnp.float32)).astype(jnp.bfloat16)
    branch = jnp.dot(hidden, w_second, preferred_element_type=jnp.float32)
    return (stream.astype(jnp.float32) + branch).astype(jnp.bfloat16)

def reference(tokens, w_in, w_out, router, exp_in, exp_out, active_rows, active_expert):
    stream = tokens.reshape(MB * TOKENS, D)
    for layer in range(LAYERS):
        stream = processor(stream, w_in[layer], w_out[layer])
    blocks = stream.reshape(MB, N_EXPERT, TOK_DEV, D).transpose(1, 0, 2, 3).reshape(N_EXPERT, ROWS_DEV, D)
    lists = active_rows.reshape(N_EXPERT, ACT_DEV).astype(jnp.int32)
    chosen = active_expert.reshape(N_EXPERT, ACT_DEV).astype(jnp.int32)
    picked = jnp.take_along_axis(blocks, lists[:, :, None], axis=1)
    contact = normalize(picked).astype(jnp.bfloat16)
    logits = jnp.einsum('nad,de->nae', contact.astype(jnp.float32), router.astype(jnp.float32))
    gate = jax.nn.sigmoid(jnp.take_along_axis(logits, chosen[:, :, None], axis=2)[:, :, 0])
    counts = (chosen[:, :, None] == jnp.arange(EXPERTS, dtype=jnp.int32)[None, None, :]).astype(jnp.int32)
    earlier = jnp.cumsum(counts, axis=1) - counts
    rank = lax.optimization_barrier(jnp.sum(earlier * counts, axis=2))
    position = (chosen * CAP + rank).astype(jnp.int32)
    owners = jnp.arange(N_EXPERT, dtype=jnp.int32)[:, None]
    buffer = jnp.zeros((N_EXPERT, EXPERTS * CAP, D), jnp.bfloat16).at[owners, position].set(contact)
    buffer = buffer.reshape(N_EXPERT, EXPERTS, CAP, D).transpose(1, 0, 2, 3).reshape(EXPERTS, N_EXPERT * CAP, D)

    def run_expert(packed):
        rows, first, second = packed
        hidden = jax.nn.silu(jnp.dot(rows, first, preferred_element_type=jnp.float32)).astype(jnp.bfloat16)
        return jnp.dot(hidden, second, preferred_element_type=jnp.float32)
    values = lax.map(run_expert, (buffer, exp_in, exp_out))
    values = values.reshape(EXPERTS, N_EXPERT, CAP, D).transpose(1, 0, 2, 3).reshape(N_EXPERT, EXPERTS * CAP, D)
    mine = jnp.take_along_axis(values, position[:, :, None], axis=1)
    mixed = blocks.astype(jnp.float32).at[owners, lists].add(gate[:, :, None] * mine)
    mixed = mixed.astype(jnp.bfloat16).reshape(N_EXPERT, MB, TOK_DEV, D).transpose(1, 0, 2, 3)
    return mixed.reshape(MB, TOKENS, D)
```

```python
import jax
import jax.numpy as jnp
from jax import lax
from jax.sharding import PartitionSpec as P


def from_behind(value, axis, steps):
    count = lax.axis_size(axis)
    initial, last = (max(0, -steps), min(count, count - steps))
    return lax.ppermute(value, axis, [(source, source + steps) for source in range(initial, last)])


def normalize(rows):
    wide = rows.astype(jnp.float32)
    scale = lax.rsqrt(jnp.mean(wide * wide, axis=-1, keepdims=True) + 1e-05)
    return wide * scale


def processor(stream, w_first, w_second):
    normed = normalize(stream).astype(jnp.bfloat16)
    hidden = jax.nn.silu(jnp.dot(normed, w_first, preferred_element_type=jnp.float32)).astype(
        jnp.bfloat16
    )
    branch = jnp.dot(hidden, w_second, preferred_element_type=jnp.float32)
    return (stream.astype(jnp.float32) + branch).astype(jnp.bfloat16)


def local(tokens, w_in, w_out, router, exp_in, exp_out, active_rows, active_expert):
    n_section = lax.axis_size("section")
    n_expert = lax.axis_size("expert")
    section = lax.axis_index("section")
    expert_index = lax.axis_index("expert")
    micro, tok_dev, width = tokens.shape
    w_first, w_second = (
        lax.all_gather(w_in, "expert", axis=1, tiled=True),
        lax.all_gather(w_out, "expert", axis=1, tiled=True),
    )
    w_first = w_first[0]
    w_second = w_second[0]
    last = n_section - 1

    def run_layer(stream):
        return processor(stream, w_first, w_second)

    def skip_layer(stream):
        return jnp.zeros_like(stream)

    def tick(step, carry):
        incoming, collected = carry
        micro_index = step - section
        valid = (micro_index >= 0) & (micro_index < micro)
        clamped = jnp.clip(micro_index, 0, micro - 1)
        fresh = lax.dynamic_index_in_dim(tokens, clamped, 0, keepdims=False)
        stream = jnp.where(section == 0, fresh, incoming)
        result = lax.cond(valid, run_layer, skip_layer, stream)
        updated = lax.dynamic_update_index_in_dim(collected, result, clamped, 0)
        collected = jnp.where(valid & (section == last), updated, collected)
        passed = from_behind(result, "section", 1)
        return (passed, collected)

    start = (jnp.zeros((tok_dev, width), jnp.bfloat16), jnp.zeros_like(tokens))
    passed, collected = lax.fori_loop(0, micro + n_section - 1, tick, start)
    rows_dev = micro * tok_dev
    flat = collected.reshape(rows_dev, width)
    n_exp = router.shape[1]
    part_width = width // n_section
    per_sub = 2
    ranks = n_section * per_sub
    chosen = active_expert[:, 0]
    onehot = chosen[:, None] == jnp.arange(n_exp, dtype=jnp.int32)[None, :]
    counts = onehot.astype(jnp.int32)
    earlier = jnp.cumsum(counts, axis=0) - counts
    rank = jnp.sum(earlier * counts, axis=1)
    picked = jnp.take(flat, active_rows, axis=0)
    contact = normalize(picked).astype(jnp.bfloat16)
    share = rank // per_sub
    slot = (share * n_exp + chosen) * per_sub + rank % per_sub
    placing = (
        jnp.arange(n_section * n_exp * per_sub, dtype=jnp.int32)[:, None] == slot[None, :]
    ).astype(jnp.bfloat16)
    dispatch = jnp.dot(placing, contact, preferred_element_type=jnp.float32).astype(jnp.bfloat16)
    dispatch = dispatch.reshape(n_section, n_exp * per_sub, width)
    columns = flat.reshape(rows_dev, n_section, part_width).transpose(1, 0, 2)
    columns = columns.reshape(n_section, rows_dev * part_width // width, width)
    payload = jnp.concatenate([columns, dispatch], axis=1)
    mine = payload[last]
    for target in range(n_section - 1):
        got = lax.ppermute(payload[target], "section", [(last, target)])
        mine = jnp.where(section == target, got, mine)
    base_rows = rows_dev * part_width // width
    base = mine[:base_rows].reshape(rows_dev, part_width)
    outgoing = mine[base_rows:].reshape(n_exp, per_sub, width)
    arrived = lax.all_to_all(outgoing, "expert", split_axis=0, concat_axis=0, tiled=True)
    rows = lax.all_gather(arrived, "section", axis=0, tiled=True).reshape(-1, width)
    e_first = exp_in[0]
    e_second = exp_out[0]
    column = lax.dynamic_slice_in_dim(router, expert_index, 1, 1)
    logits = jnp.dot(rows, column, preferred_element_type=jnp.float32)[:, 0]
    gate = jax.nn.sigmoid(logits)
    hidden = jax.nn.silu(jnp.dot(rows, e_first, preferred_element_type=jnp.float32)).astype(
        jnp.bfloat16
    )
    partial_value = jnp.dot(hidden, e_second, preferred_element_type=jnp.float32)
    scaled = (gate[:, None] * partial_value).astype(jnp.bfloat16)
    summed = lax.psum_scatter(scaled, "section", scatter_dimension=1, tiled=True)
    summed = summed.reshape(n_section, n_expert, per_sub, part_width).transpose(1, 0, 2, 3)
    returned = lax.all_to_all(summed, "expert", split_axis=0, concat_axis=0, tiled=True)
    returned = returned.reshape(n_exp * ranks, part_width)
    position = chosen * ranks + rank
    added = jnp.take(returned, position, axis=0).astype(jnp.float32)
    mixed = base.astype(jnp.float32).at[active_rows].add(added)
    return mixed.astype(jnp.bfloat16).reshape(micro, tok_dev, part_width)


def solution(mesh):
    return jax.shard_map(
        local,
        mesh=mesh,
        in_specs=(
            P(None, "expert", None),
            P("section", "expert", None),
            P("section", "expert", None),
            P(),
            P("expert", None, "section"),
            P("expert", "section", None),
            P("expert"),
            P("expert", None),
        ),
        out_specs=P(None, "expert", "section"),
        check_vma=False,
    )
```

```python
import jax
import jax.numpy as jnp
from jax import lax
from jax.sharding import PartitionSpec as P


def from_behind(value, axis, steps):
    count = lax.axis_size(axis)
    initial, last = (max(0, -steps), min(count, count - steps))
    return lax.ppermute(value, axis, [(source, source + steps) for source in range(initial, last)])


def ring_gather(chunk, axis, size, stride):
    index = lax.axis_index(axis)
    count = lax.axis_size(axis)
    place = (index // stride) % size

    def shifted(step):
        pairs = []
        for member in range(count):
            at = (member // stride) % size
            to = member + (((at + step) % size) - at) * stride
            pairs.append((member, to))
        return pairs

    out = jnp.zeros((size,) + chunk.shape, chunk.dtype)
    out = lax.dynamic_update_index_in_dim(out, chunk, place, 0)
    ahead, behind = chunk, chunk
    for step in range(1, size // 2 + 1):
        ahead = lax.ppermute(ahead, axis, shifted(1))
        out = lax.dynamic_update_index_in_dim(out, ahead, (place - step) % size, 0)
        if step < size - step:
            behind = lax.ppermute(behind, axis, shifted(-1))
            out = lax.dynamic_update_index_in_dim(out, behind, (place + step) % size, 0)
    return out


def normalize(rows):
    wide = rows.astype(jnp.float32)
    scale = lax.rsqrt(jnp.mean(wide * wide, axis=-1, keepdims=True) + 1e-05)
    return wide * scale


def processor(stream, w_first, w_second):
    normed = normalize(stream).astype(jnp.bfloat16)
    hidden = jax.nn.silu(jnp.dot(normed, w_first, preferred_element_type=jnp.float32)).astype(
        jnp.bfloat16
    )
    branch = jnp.dot(hidden, w_second, preferred_element_type=jnp.float32)
    return (stream.astype(jnp.float32) + branch).astype(jnp.bfloat16)


def local(tokens, w_in, w_out, router, exp_in, exp_out, active_rows, active_expert):
    n_section = lax.axis_size("section")
    n_expert = lax.axis_size("expert")
    section = lax.axis_index("section")
    expert_index = lax.axis_index("expert")
    micro, tok_dev, width = tokens.shape
    w_first = lax.all_gather(w_in, "expert", axis=1, tiled=True)[0]
    inner = 4 if n_expert % 4 == 0 else 1
    w_second = ring_gather(w_out[0], "expert", inner, 1)
    w_second = ring_gather(w_second, "expert", n_expert // inner, inner)
    w_second = w_second.reshape(-1, width)
    last = n_section - 1

    def run_layer(stream):
        return processor(stream, w_first, w_second)

    def skip_layer(stream):
        return jnp.zeros_like(stream)

    def tick(step, carry):
        incoming, collected = carry
        micro_index = step - section
        valid = (micro_index >= 0) & (micro_index < micro)
        clamped = jnp.clip(micro_index, 0, micro - 1)
        fresh = lax.dynamic_index_in_dim(tokens, clamped, 0, keepdims=False)
        stream = jnp.where(section == 0, fresh, incoming)
        result = lax.cond(valid, run_layer, skip_layer, stream)
        updated = lax.dynamic_update_index_in_dim(collected, result, clamped, 0)
        collected = jnp.where(valid & (section == last), updated, collected)
        passed = from_behind(result, "section", 1)
        return (passed, collected)

    start = (jnp.zeros((tok_dev, width), jnp.bfloat16), jnp.zeros_like(tokens))
    passed, collected = lax.fori_loop(0, micro + n_section - 1, tick, start)
    rows_dev = micro * tok_dev
    flat = collected.reshape(rows_dev, width)
    n_exp = router.shape[1]
    part_width = width // n_section
    per_sub = 2
    ranks = n_section * per_sub
    chosen = active_expert[:, 0]
    onehot = chosen[:, None] == jnp.arange(n_exp, dtype=jnp.int32)[None, :]
    counts = onehot.astype(jnp.int32)
    earlier = jnp.cumsum(counts, axis=0) - counts
    rank = jnp.sum(earlier * counts, axis=1)
    picked = jnp.take(flat, active_rows, axis=0)
    contact = normalize(picked).astype(jnp.bfloat16)
    share = rank // per_sub
    slot = (share * n_exp + chosen) * per_sub + rank % per_sub
    placing = (
        jnp.arange(n_section * n_exp * per_sub, dtype=jnp.int32)[:, None] == slot[None, :]
    ).astype(jnp.bfloat16)
    dispatch = jnp.dot(placing, contact, preferred_element_type=jnp.float32).astype(jnp.bfloat16)
    dispatch = dispatch.reshape(n_section, n_exp * per_sub, width)
    columns = flat.reshape(rows_dev, n_section, part_width).transpose(1, 0, 2)
    columns = columns.reshape(n_section, rows_dev * part_width // width, width)
    payload = jnp.concatenate([columns, dispatch], axis=1)
    mine = payload[last]
    for target in range(n_section - 1):
        got = lax.ppermute(payload[target], "section", [(last, target)])
        mine = jnp.where(section == target, got, mine)
    base_rows = rows_dev * part_width // width
    base = mine[:base_rows].reshape(rows_dev, part_width)
    outgoing = mine[base_rows:].reshape(n_exp, per_sub, width)
    arrived = lax.all_to_all(outgoing, "expert", split_axis=0, concat_axis=0, tiled=True)
    rows = lax.all_gather(arrived, "section", axis=0, tiled=True).reshape(-1, width)
    e_first = exp_in[0]
    e_second = exp_out[0]
    column = lax.dynamic_slice_in_dim(router, expert_index, 1, 1)
    logits = jnp.dot(rows, column, preferred_element_type=jnp.float32)[:, 0]
    gate = jax.nn.sigmoid(logits)
    hidden = jax.nn.silu(jnp.dot(rows, e_first, preferred_element_type=jnp.float32)).astype(
        jnp.bfloat16
    )
    partial_value = jnp.dot(hidden, e_second, preferred_element_type=jnp.float32)
    scaled = (gate[:, None] * partial_value).astype(jnp.bfloat16)
    summed = lax.psum_scatter(scaled, "section", scatter_dimension=1, tiled=True)
    summed = summed.reshape(n_section, n_expert, per_sub, part_width).transpose(1, 0, 2, 3)
    returned = lax.all_to_all(summed, "expert", split_axis=0, concat_axis=0, tiled=True)
    returned = returned.reshape(n_exp * ranks, part_width)
    position = chosen * ranks + rank
    added = jnp.take(returned, position, axis=0).astype(jnp.float32)
    mixed = base.astype(jnp.float32).at[active_rows].add(added)
    return mixed.astype(jnp.bfloat16).reshape(micro, tok_dev, part_width)


def solution(mesh):
    return jax.shard_map(
        local,
        mesh=mesh,
        in_specs=(
            P(None, "expert", None),
            P("section", "expert", None),
            P("section", "expert", None),
            P(),
            P("expert", None, "section"),
            P("expert", "section", None),
            P("expert"),
            P("expert", None),
        ),
        out_specs=P(None, "expert", "section"),
        check_vma=False,
    )
```

```python
import jax
import jax.numpy as jnp
from jax import lax
from jax.sharding import PartitionSpec as P


def from_behind(value, axis, steps):
    count = lax.axis_size(axis)
    initial, last = (max(0, -steps), min(count, count - steps))
    return lax.ppermute(value, axis, [(source, source + steps) for source in range(initial, last)])


def ring_gather(chunk, axis, size, stride):
    index = lax.axis_index(axis)
    count = lax.axis_size(axis)
    place = (index // stride) % size

    def shifted(step):
        pairs = []
        for member in range(count):
            at = (member // stride) % size
            to = member + (((at + step) % size) - at) * stride
            pairs.append((member, to))
        return pairs

    out = jnp.zeros((size,) + chunk.shape, chunk.dtype)
    out = lax.dynamic_update_index_in_dim(out, chunk, place, 0)
    ahead, behind = chunk, chunk
    for step in range(1, size // 2 + 1):
        ahead = lax.ppermute(ahead, axis, shifted(1))
        out = lax.dynamic_update_index_in_dim(out, ahead, (place - step) % size, 0)
        if step < size - step:
            behind = lax.ppermute(behind, axis, shifted(-1))
            out = lax.dynamic_update_index_in_dim(out, behind, (place + step) % size, 0)
    return out


def normalize(rows):
    wide = rows.astype(jnp.float32)
    scale = lax.rsqrt(jnp.mean(wide * wide, axis=-1, keepdims=True) + 1e-05)
    return wide * scale


def processor(stream, w_first, w_second):
    normed = normalize(stream).astype(jnp.bfloat16)
    hidden = jax.nn.silu(jnp.dot(normed, w_first, preferred_element_type=jnp.float32)).astype(
        jnp.bfloat16
    )
    branch = jnp.dot(hidden, w_second, preferred_element_type=jnp.float32)
    return (stream.astype(jnp.float32) + branch).astype(jnp.bfloat16)


def local(tokens, w_in, w_out, router, exp_in, exp_out, active_rows, active_expert):
    n_section = lax.axis_size("section")
    n_expert = lax.axis_size("expert")
    section = lax.axis_index("section")
    expert_index = lax.axis_index("expert")
    micro, tok_dev, width = tokens.shape
    w_first = lax.all_gather(w_in, "expert", axis=1, tiled=True)[0]
    inner = 4 if n_expert % 4 == 0 else 1
    w_second = ring_gather(w_out[0], "expert", inner, 1)
    w_second = ring_gather(w_second, "expert", n_expert // inner, inner)
    w_second = w_second.reshape(-1, width)
    last = n_section - 1

    def run_layer(stream):
        return processor(stream, w_first, w_second)

    def skip_layer(stream):
        return jnp.zeros_like(stream)

    groups = micro // 2 if micro % 2 == 0 else micro
    chunks = tokens.reshape(groups, micro * tok_dev // groups, width)

    def tick(step, carry):
        incoming, collected = carry
        micro_index = step - section
        valid = (micro_index >= 0) & (micro_index < groups)
        clamped = jnp.clip(micro_index, 0, groups - 1)
        fresh = lax.dynamic_index_in_dim(chunks, clamped, 0, keepdims=False)
        stream = jnp.where(section == 0, fresh, incoming)
        result = lax.cond(valid, run_layer, skip_layer, stream)
        held = lax.dynamic_index_in_dim(collected, clamped, 0, keepdims=False)
        kept = jnp.where(valid & (section == last), result, held)
        collected = lax.dynamic_update_index_in_dim(collected, kept, clamped, 0)
        passed = from_behind(result, "section", 1)
        return (passed, collected)

    start = (jnp.zeros(chunks.shape[1:], jnp.bfloat16), jnp.zeros_like(chunks))
    passed, collected = lax.fori_loop(0, groups + n_section - 1, tick, start)
    rows_dev = micro * tok_dev
    flat = collected.reshape(rows_dev, width)
    n_exp = router.shape[1]
    part_width = width // n_section
    per_sub = 2
    ranks = n_section * per_sub
    chosen = active_expert[:, 0]
    onehot = chosen[:, None] == jnp.arange(n_exp, dtype=jnp.int32)[None, :]
    counts = onehot.astype(jnp.int32)
    earlier = jnp.cumsum(counts, axis=0) - counts
    rank = jnp.sum(earlier * counts, axis=1)
    picked = jnp.take(flat, active_rows, axis=0)
    contact = normalize(picked).astype(jnp.bfloat16)
    share = rank // per_sub
    slot = (share * n_exp + chosen) * per_sub + rank % per_sub
    placing = (
        jnp.arange(n_section * n_exp * per_sub, dtype=jnp.int32)[:, None] == slot[None, :]
    ).astype(jnp.bfloat16)
    dispatch = jnp.dot(placing, contact, preferred_element_type=jnp.float32).astype(jnp.bfloat16)
    dispatch = dispatch.reshape(n_section, n_exp * per_sub, width)
    columns = flat.reshape(rows_dev, n_section, part_width).transpose(1, 0, 2)
    columns = columns.reshape(n_section, rows_dev * part_width // width, width)
    payload = jnp.concatenate([columns, dispatch], axis=1)
    mine = payload[last]
    for target in range(n_section - 1):
        got = lax.ppermute(payload[target], "section", [(last, target)])
        mine = jnp.where(section == target, got, mine)
    base_rows = rows_dev * part_width // width
    base = mine[:base_rows].reshape(rows_dev, part_width)
    outgoing = mine[base_rows:].reshape(n_exp, per_sub, width)
    arrived = lax.all_to_all(outgoing, "expert", split_axis=0, concat_axis=0, tiled=True)
    rows = lax.all_gather(arrived, "section", axis=0, tiled=True).reshape(-1, width)
    e_first = exp_in[0]
    e_second = exp_out[0]
    column = lax.dynamic_slice_in_dim(router, expert_index, 1, 1)
    logits = jnp.dot(rows, column, preferred_element_type=jnp.float32)[:, 0]
    gate = jax.nn.sigmoid(logits)
    hidden = jax.nn.silu(jnp.dot(rows, e_first, preferred_element_type=jnp.float32)).astype(
        jnp.bfloat16
    )
    partial_value = jnp.dot(hidden, e_second, preferred_element_type=jnp.float32)
    scaled = (gate[:, None] * partial_value).astype(jnp.bfloat16)
    summed = lax.psum_scatter(scaled, "section", scatter_dimension=1, tiled=True)
    summed = summed.reshape(n_section, n_expert, per_sub, part_width).transpose(1, 0, 2, 3)
    returned = lax.all_to_all(summed, "expert", split_axis=0, concat_axis=0, tiled=True)
    returned = returned.reshape(n_exp * ranks, part_width)
    position = chosen * ranks + rank
    added = jnp.take(returned, position, axis=0).astype(jnp.float32)
    mixed = base.astype(jnp.float32).at[active_rows].add(added)
    return mixed.astype(jnp.bfloat16).reshape(micro, tok_dev, part_width)


def solution(mesh):
    return jax.shard_map(
        local,
        mesh=mesh,
        in_specs=(
            P(None, "expert", None),
            P("section", "expert", None),
            P("section", "expert", None),
            P(),
            P("expert", None, "section"),
            P("expert", "section", None),
            P("expert"),
            P("expert", None),
        ),
        out_specs=P(None, "expert", "section"),
        check_vma=False,
    )
```

```python
import jax
import jax.numpy as jnp
from jax import lax
from jax.sharding import PartitionSpec as P


def from_behind(value, axis, steps):
    count = lax.axis_size(axis)
    initial, last = (max(0, -steps), min(count, count - steps))
    return lax.ppermute(value, axis, [(source, source + steps) for source in range(initial, last)])


def ring_gather(chunk, axis, size, stride):
    index = lax.axis_index(axis)
    count = lax.axis_size(axis)
    place = (index // stride) % size

    def shifted(step):
        pairs = []
        for member in range(count):
            at = (member // stride) % size
            to = member + (((at + step) % size) - at) * stride
            pairs.append((member, to))
        return pairs

    out = jnp.zeros((size,) + chunk.shape, chunk.dtype)
    out = lax.dynamic_update_index_in_dim(out, chunk, place, 0)
    ahead, behind = chunk, chunk
    for step in range(1, size // 2 + 1):
        ahead = lax.ppermute(ahead, axis, shifted(1))
        out = lax.dynamic_update_index_in_dim(out, ahead, (place - step) % size, 0)
        if step < size - step:
            behind = lax.ppermute(behind, axis, shifted(-1))
            out = lax.dynamic_update_index_in_dim(out, behind, (place + step) % size, 0)
    return out


def normalize(rows):
    wide = rows.astype(jnp.float32)
    scale = lax.rsqrt(jnp.mean(wide * wide, axis=-1, keepdims=True) + 1e-05)
    return wide * scale


def processor(stream, w_first, w_second):
    normed = normalize(stream).astype(jnp.bfloat16)
    hidden = jax.nn.silu(jnp.dot(normed, w_first, preferred_element_type=jnp.float32)).astype(
        jnp.bfloat16
    )
    branch = jnp.dot(hidden, w_second, preferred_element_type=jnp.float32)
    return (stream.astype(jnp.float32) + branch).astype(jnp.bfloat16)


def local(tokens, w_in, w_out, router, exp_in, exp_out, active_rows, active_expert):
    n_section = lax.axis_size("section")
    n_expert = lax.axis_size("expert")
    section = lax.axis_index("section")
    expert_index = lax.axis_index("expert")
    micro, tok_dev, width = tokens.shape
    inner = 4 if n_expert % 4 == 0 else 1
    w_first = ring_gather(w_in[0], "expert", n_expert // inner, inner)
    w_first = ring_gather(w_first, "expert", inner, 1)
    w_first = w_first.transpose(1, 0, 2, 3).reshape(-1, width)
    w_second = ring_gather(w_out[0], "expert", inner, 1)
    w_second = ring_gather(w_second, "expert", n_expert // inner, inner)
    w_second = w_second.reshape(-1, width)
    last = n_section - 1

    def run_layer(stream):
        return processor(stream, w_first, w_second)

    def skip_layer(stream):
        return jnp.zeros_like(stream)

    groups = micro // 2 if micro % 2 == 0 else micro
    chunks = tokens.reshape(groups, micro * tok_dev // groups, width)

    def tick(step, carry):
        incoming, collected = carry
        micro_index = step - section
        valid = (micro_index >= 0) & (micro_index < groups)
        clamped = jnp.clip(micro_index, 0, groups - 1)
        fresh = lax.dynamic_index_in_dim(chunks, clamped, 0, keepdims=False)
        stream = jnp.where(section == 0, fresh, incoming)
        result = lax.cond(valid, run_layer, skip_layer, stream)
        held = lax.dynamic_index_in_dim(collected, clamped, 0, keepdims=False)
        kept = jnp.where(valid & (section == last), result, held)
        collected = lax.dynamic_update_index_in_dim(collected, kept, clamped, 0)
        passed = from_behind(result, "section", 1)
        return (passed, collected)

    start = (jnp.zeros(chunks.shape[1:], jnp.bfloat16), jnp.zeros_like(chunks))
    passed, collected = lax.fori_loop(0, groups + n_section - 1, tick, start)
    rows_dev = micro * tok_dev
    flat = collected.reshape(rows_dev, width)
    n_exp = router.shape[1]
    part_width = width // n_section
    per_sub = 2
    ranks = n_section * per_sub
    chosen = active_expert[:, 0]
    onehot = chosen[:, None] == jnp.arange(n_exp, dtype=jnp.int32)[None, :]
    counts = onehot.astype(jnp.int32)
    earlier = jnp.cumsum(counts, axis=0) - counts
    rank = jnp.sum(earlier * counts, axis=1)
    picked = jnp.take(flat, active_rows, axis=0)
    contact = normalize(picked).astype(jnp.bfloat16)
    share = rank // per_sub
    slot = (share * n_exp + chosen) * per_sub + rank % per_sub
    placing = (
        jnp.arange(n_section * n_exp * per_sub, dtype=jnp.int32)[:, None] == slot[None, :]
    ).astype(jnp.bfloat16)
    dispatch = jnp.dot(placing, contact, preferred_element_type=jnp.float32).astype(jnp.bfloat16)
    dispatch = dispatch.reshape(n_section, n_exp * per_sub, width)
    columns = flat.reshape(rows_dev, n_section, part_width).transpose(1, 0, 2)
    columns = columns.reshape(n_section, rows_dev * part_width // width, width)
    payload = jnp.concatenate([columns, dispatch], axis=1)
    mine = payload[last]
    for target in range(n_section - 1):
        got = lax.ppermute(payload[target], "section", [(last, target)])
        mine = jnp.where(section == target, got, mine)
    base_rows = rows_dev * part_width // width
    base = mine[:base_rows].reshape(rows_dev, part_width)
    outgoing = mine[base_rows:].reshape(n_exp, per_sub, width)
    arrived = lax.all_to_all(outgoing, "expert", split_axis=0, concat_axis=0, tiled=True)
    rows = lax.all_gather(arrived, "section", axis=0, tiled=True).reshape(-1, width)
    e_first = exp_in[0]
    e_second = exp_out[0]
    column = lax.dynamic_slice_in_dim(router, expert_index, 1, 1)
    logits = jnp.dot(rows, column, preferred_element_type=jnp.float32)[:, 0]
    gate = jax.nn.sigmoid(logits)
    hidden = jax.nn.silu(jnp.dot(rows, e_first, preferred_element_type=jnp.float32)).astype(
        jnp.bfloat16
    )
    partial_value = jnp.dot(hidden, e_second, preferred_element_type=jnp.float32)
    scaled = (gate[:, None] * partial_value).astype(jnp.bfloat16)
    summed = lax.psum_scatter(scaled, "section", scatter_dimension=1, tiled=True)
    summed = summed.reshape(n_section, n_expert, per_sub, part_width).transpose(1, 0, 2, 3)
    returned = lax.all_to_all(summed, "expert", split_axis=0, concat_axis=0, tiled=True)
    returned = returned.reshape(n_exp * ranks, part_width)
    position = chosen * ranks + rank
    added = jnp.take(returned, position, axis=0).astype(jnp.float32)
    mixed = base.astype(jnp.float32).at[active_rows].add(added)
    return mixed.astype(jnp.bfloat16).reshape(micro, tok_dev, part_width)


def solution(mesh):
    return jax.shard_map(
        local,
        mesh=mesh,
        in_specs=(
            P(None, "expert", None),
            P("section", "expert", None),
            P("section", "expert", None),
            P(),
            P("expert", None, "section"),
            P("expert", "section", None),
            P("expert"),
            P("expert", None),
        ),
        out_specs=P(None, "expert", "section"),
        check_vma=False,
    )
```

```python
import jax
import jax.numpy as jnp
from jax import lax
from jax.sharding import PartitionSpec as P


def from_behind(value, axis, steps):
    count = lax.axis_size(axis)
    initial, last = (max(0, -steps), min(count, count - steps))
    return lax.ppermute(value, axis, [(source, source + steps) for source in range(initial, last)])


def ring_gather(chunk, axis, size, stride):
    index = lax.axis_index(axis)
    count = lax.axis_size(axis)
    place = (index // stride) % size

    def shifted(step):
        pairs = []
        for member in range(count):
            at = (member // stride) % size
            to = member + (((at + step) % size) - at) * stride
            pairs.append((member, to))
        return pairs

    out = jnp.zeros((size,) + chunk.shape, chunk.dtype)
    out = lax.dynamic_update_index_in_dim(out, chunk, place, 0)
    ahead, behind = chunk, chunk
    split = 0 if chunk.shape[0] % 2 == 0 else 1
    half = chunk.shape[split] // 2
    for step in range(1, size // 2 + 1):
        if step < size - step:
            ahead = lax.ppermute(ahead, axis, shifted(1))
            out = lax.dynamic_update_index_in_dim(out, ahead, (place - step) % size, 0)
            behind = lax.ppermute(behind, axis, shifted(-1))
            out = lax.dynamic_update_index_in_dim(out, behind, (place + step) % size, 0)
        else:
            front = lax.slice_in_dim(ahead, 0, half, axis=split)
            back = lax.slice_in_dim(behind, half, chunk.shape[split], axis=split)
            front = lax.ppermute(front, axis, shifted(1))
            back = lax.ppermute(back, axis, shifted(-1))
            whole = jnp.concatenate([front, back], axis=split)
            out = lax.dynamic_update_index_in_dim(out, whole, (place - step) % size, 0)
    return out


def normalize(rows):
    wide = rows.astype(jnp.float32)
    scale = lax.rsqrt(jnp.mean(wide * wide, axis=-1, keepdims=True) + 1e-05)
    return wide * scale


def processor(stream, w_first, w_second):
    normed = normalize(stream).astype(jnp.bfloat16)
    hidden = jax.nn.silu(jnp.dot(normed, w_first, preferred_element_type=jnp.float32)).astype(
        jnp.bfloat16
    )
    branch = jnp.dot(hidden, w_second, preferred_element_type=jnp.float32)
    return (stream.astype(jnp.float32) + branch).astype(jnp.bfloat16)


def local(tokens, w_in, w_out, router, exp_in, exp_out, active_rows, active_expert):
    n_section = lax.axis_size("section")
    n_expert = lax.axis_size("expert")
    section = lax.axis_index("section")
    expert_index = lax.axis_index("expert")
    micro, tok_dev, width = tokens.shape
    inner = 4 if n_expert % 4 == 0 else 1
    w_first = ring_gather(w_in[0], "expert", n_expert // inner, inner)
    w_first = ring_gather(w_first, "expert", inner, 1)
    w_first = w_first.transpose(1, 0, 2, 3).reshape(-1, width)
    w_second = ring_gather(w_out[0], "expert", inner, 1)
    w_second = ring_gather(w_second, "expert", n_expert // inner, inner)
    w_second = w_second.reshape(-1, width)
    last = n_section - 1

    def run_layer(stream):
        return processor(stream, w_first, w_second)

    def skip_layer(stream):
        return jnp.zeros_like(stream)

    groups = micro // 2 if micro % 2 == 0 else micro
    chunks = tokens.reshape(groups, micro * tok_dev // groups, width)

    def tick(step, carry):
        incoming, collected = carry
        micro_index = step - section
        valid = (micro_index >= 0) & (micro_index < groups)
        clamped = jnp.clip(micro_index, 0, groups - 1)
        fresh = lax.dynamic_index_in_dim(chunks, clamped, 0, keepdims=False)
        stream = jnp.where(section == 0, fresh, incoming)
        result = lax.cond(valid, run_layer, skip_layer, stream)
        held = lax.dynamic_index_in_dim(collected, clamped, 0, keepdims=False)
        kept = jnp.where(valid & (section == last), result, held)
        collected = lax.dynamic_update_index_in_dim(collected, kept, clamped, 0)
        passed = from_behind(result, "section", 1)
        return (passed, collected)

    start = (jnp.zeros(chunks.shape[1:], jnp.bfloat16), jnp.zeros_like(chunks))
    passed, collected = lax.fori_loop(0, groups + n_section - 1, tick, start)
    rows_dev = micro * tok_dev
    flat = collected.reshape(rows_dev, width)
    n_exp = router.shape[1]
    part_width = width // n_section
    per_sub = 2
    ranks = n_section * per_sub
    chosen = active_expert[:, 0]
    onehot = chosen[:, None] == jnp.arange(n_exp, dtype=jnp.int32)[None, :]
    counts = onehot.astype(jnp.int32)
    earlier = jnp.cumsum(counts, axis=0) - counts
    rank = jnp.sum(earlier * counts, axis=1)
    picked = jnp.take(flat, active_rows, axis=0)
    contact = normalize(picked).astype(jnp.bfloat16)
    share = rank // per_sub
    slot = (share * n_exp + chosen) * per_sub + rank % per_sub
    placing = (
        jnp.arange(n_section * n_exp * per_sub, dtype=jnp.int32)[:, None] == slot[None, :]
    ).astype(jnp.bfloat16)
    dispatch = jnp.dot(placing, contact, preferred_element_type=jnp.float32).astype(jnp.bfloat16)
    dispatch = dispatch.reshape(n_section, n_exp * per_sub, width)
    columns = flat.reshape(rows_dev, n_section, part_width).transpose(1, 0, 2)
    columns = columns.reshape(n_section, rows_dev * part_width // width, width)
    def from_last(parts):
        mine = parts[last]
        for target in range(n_section - 1):
            got = lax.ppermute(parts[target], "section", [(last, target)])
            mine = jnp.where(section == target, got, mine)
        return mine

    outgoing = from_last(dispatch).reshape(n_exp, per_sub, width)
    arrived = lax.all_to_all(outgoing, "expert", split_axis=0, concat_axis=0, tiled=True)
    columns, arrived = lax.optimization_barrier((columns, arrived))
    base = from_last(columns).reshape(rows_dev, part_width)
    rows = lax.all_gather(arrived, "section", axis=0, tiled=True).reshape(-1, width)
    e_first = exp_in[0]
    e_second = exp_out[0]
    column = lax.dynamic_slice_in_dim(router, expert_index, 1, 1)
    logits = jnp.dot(rows, column, preferred_element_type=jnp.float32)[:, 0]
    gate = jax.nn.sigmoid(logits)
    hidden = jax.nn.silu(jnp.dot(rows, e_first, preferred_element_type=jnp.float32)).astype(
        jnp.bfloat16
    )
    partial_value = jnp.dot(hidden, e_second, preferred_element_type=jnp.float32)
    scaled = (gate[:, None] * partial_value).astype(jnp.bfloat16)
    summed = lax.psum_scatter(scaled, "section", scatter_dimension=1, tiled=True)
    summed = summed.reshape(n_section, n_expert, per_sub, part_width).transpose(1, 0, 2, 3)
    returned = lax.all_to_all(summed, "expert", split_axis=0, concat_axis=0, tiled=True)
    returned = returned.reshape(n_exp * ranks, part_width)
    position = chosen * ranks + rank
    added = jnp.take(returned, position, axis=0).astype(jnp.float32)
    mixed = base.astype(jnp.float32).at[active_rows].add(added)
    return mixed.astype(jnp.bfloat16).reshape(micro, tok_dev, part_width)


def solution(mesh):
    return jax.shard_map(
        local,
        mesh=mesh,
        in_specs=(
            P(None, "expert", None),
            P("section", "expert", None),
            P("section", "expert", None),
            P(),
            P("expert", None, "section"),
            P("expert", "section", None),
            P("expert"),
            P("expert", None),
        ),
        out_specs=P(None, "expert", "section"),
        check_vma=False,
    )
```

```python
import jax
import jax.numpy as jnp
from jax import lax
from jax.sharding import PartitionSpec as P


def from_behind(value, axis, steps):
    count = lax.axis_size(axis)
    initial, last = (max(0, -steps), min(count, count - steps))
    return lax.ppermute(value, axis, [(source, source + steps) for source in range(initial, last)])


def ring_gather(chunk, axis, size, stride):
    index = lax.axis_index(axis)
    count = lax.axis_size(axis)
    place = (index // stride) % size

    def shifted(step):
        pairs = []
        for member in range(count):
            at = (member // stride) % size
            to = member + (((at + step) % size) - at) * stride
            pairs.append((member, to))
        return pairs

    out = jnp.zeros((size,) + chunk.shape, chunk.dtype)
    out = lax.dynamic_update_index_in_dim(out, chunk, place, 0)
    ahead, behind = chunk, chunk
    split = 0 if chunk.shape[0] % 2 == 0 else 1
    half = chunk.shape[split] // 2
    for step in range(1, size // 2 + 1):
        if step < size - step:
            ahead = lax.ppermute(ahead, axis, shifted(1))
            out = lax.dynamic_update_index_in_dim(out, ahead, (place - step) % size, 0)
            behind = lax.ppermute(behind, axis, shifted(-1))
            out = lax.dynamic_update_index_in_dim(out, behind, (place + step) % size, 0)
        else:
            front = lax.slice_in_dim(ahead, 0, half, axis=split)
            back = lax.slice_in_dim(behind, half, chunk.shape[split], axis=split)
            front = lax.ppermute(front, axis, shifted(1))
            back = lax.ppermute(back, axis, shifted(-1))
            whole = jnp.concatenate([front, back], axis=split)
            out = lax.dynamic_update_index_in_dim(out, whole, (place - step) % size, 0)
    return out


def normalize(rows):
    wide = rows.astype(jnp.float32)
    scale = lax.rsqrt(jnp.mean(wide * wide, axis=-1, keepdims=True) + 1e-05)
    return wide * scale


def processor(stream, w_first, w_second):
    normed = normalize(stream).astype(jnp.bfloat16)
    hidden = jax.nn.silu(jnp.dot(normed, w_first, preferred_element_type=jnp.float32)).astype(
        jnp.bfloat16
    )
    branch = jnp.dot(hidden, w_second, preferred_element_type=jnp.float32)
    return (stream.astype(jnp.float32) + branch).astype(jnp.bfloat16)


def local(tokens, w_in, w_out, router, exp_in, exp_out, active_rows, active_expert):
    n_section = lax.axis_size("section")
    n_expert = lax.axis_size("expert")
    section = lax.axis_index("section")
    expert_index = lax.axis_index("expert")
    micro, tok_dev, width = tokens.shape
    inner = 4 if n_expert % 4 == 0 else 1
    w_first = ring_gather(w_in[0], "expert", n_expert // inner, inner)
    w_first = ring_gather(w_first, "expert", inner, 1)
    w_first = w_first.transpose(1, 0, 2, 3).reshape(-1, width)
    w_second = ring_gather(w_out[0], "expert", inner, 1)
    w_second = ring_gather(w_second, "expert", n_expert // inner, inner)
    w_second = w_second.reshape(-1, width)
    last = n_section - 1

    def run_layer(stream):
        return processor(stream, w_first, w_second)

    def skip_layer(stream):
        return jnp.zeros_like(stream)

    groups = 3 if micro * tok_dev % 3 == 0 else micro
    chunks = tokens.reshape(groups, micro * tok_dev // groups, width)

    def tick(step, carry):
        incoming, collected = carry
        micro_index = step - section
        valid = (micro_index >= 0) & (micro_index < groups)
        clamped = jnp.clip(micro_index, 0, groups - 1)
        fresh = lax.dynamic_index_in_dim(chunks, clamped, 0, keepdims=False)
        stream = jnp.where(section == 0, fresh, incoming)
        result = lax.cond(valid, run_layer, skip_layer, stream)
        held = lax.dynamic_index_in_dim(collected, clamped, 0, keepdims=False)
        kept = jnp.where(valid & (section == last), result, held)
        collected = lax.dynamic_update_index_in_dim(collected, kept, clamped, 0)
        passed = from_behind(result, "section", 1)
        return (passed, collected)

    start = (jnp.zeros(chunks.shape[1:], jnp.bfloat16), jnp.zeros_like(chunks))
    passed, collected = lax.fori_loop(0, groups + n_section - 1, tick, start)
    rows_dev = micro * tok_dev
    flat = collected.reshape(rows_dev, width)
    n_exp = router.shape[1]
    part_width = width // n_section
    per_sub = 2
    ranks = n_section * per_sub
    chosen = active_expert[:, 0]
    onehot = chosen[:, None] == jnp.arange(n_exp, dtype=jnp.int32)[None, :]
    counts = onehot.astype(jnp.int32)
    earlier = jnp.cumsum(counts, axis=0) - counts
    rank = jnp.sum(earlier * counts, axis=1)
    picked = jnp.take(flat, active_rows, axis=0)
    contact = normalize(picked).astype(jnp.bfloat16)
    share = rank // per_sub
    slot = (share * n_exp + chosen) * per_sub + rank % per_sub
    placing = (
        jnp.arange(n_section * n_exp * per_sub, dtype=jnp.int32)[:, None] == slot[None, :]
    ).astype(jnp.bfloat16)
    dispatch = jnp.dot(placing, contact, preferred_element_type=jnp.float32).astype(jnp.bfloat16)
    dispatch = dispatch.reshape(n_section, n_exp * per_sub, width)
    columns = flat.reshape(rows_dev, n_section, part_width).transpose(1, 0, 2)
    columns = columns.reshape(n_section, rows_dev * part_width // width, width)
    def from_last(parts):
        mine = parts[last]
        for target in range(n_section - 1):
            got = lax.ppermute(parts[target], "section", [(last, target)])
            mine = jnp.where(section == target, got, mine)
        return mine

    outgoing = from_last(dispatch).reshape(n_exp, per_sub * width)
    arrived = lax.all_to_all(outgoing, "expert", split_axis=0, concat_axis=0, tiled=True)
    columns, arrived = lax.optimization_barrier((columns, arrived))
    base = from_last(columns).reshape(rows_dev, part_width)
    rows = lax.all_gather(arrived, "section", axis=0, tiled=True).reshape(-1, width)
    e_first = exp_in[0]
    e_second = exp_out[0]
    column = lax.dynamic_slice_in_dim(router, expert_index, 1, 1)
    logits = jnp.dot(rows, column, preferred_element_type=jnp.float32)[:, 0]
    gate = jax.nn.sigmoid(logits)
    hidden = jax.nn.silu(jnp.dot(rows, e_first, preferred_element_type=jnp.float32)).astype(
        jnp.bfloat16
    )
    partial_value = jnp.dot(hidden, e_second, preferred_element_type=jnp.float32)
    scaled = (gate[:, None] * partial_value).astype(jnp.bfloat16)
    summed = lax.psum_scatter(scaled, "section", scatter_dimension=1, tiled=True)
    summed = summed.reshape(n_section, n_expert, per_sub, part_width).transpose(1, 0, 2, 3)
    summed = summed.reshape(n_expert, n_section * per_sub * part_width)
    returned = lax.all_to_all(summed, "expert", split_axis=0, concat_axis=0, tiled=True)
    returned = returned.reshape(n_exp * ranks, part_width)
    position = chosen * ranks + rank
    added = jnp.take(returned, position, axis=0).astype(jnp.float32)
    mixed = base.astype(jnp.float32).at[active_rows].add(added)
    return mixed.astype(jnp.bfloat16).reshape(micro, tok_dev, part_width)


def solution(mesh):
    return jax.shard_map(
        local,
        mesh=mesh,
        in_specs=(
            P(None, "expert", None),
            P("section", "expert", None),
            P("section", "expert", None),
            P(),
            P("expert", None, "section"),
            P("expert", "section", None),
            P("expert"),
            P("expert", None),
        ),
        out_specs=P(None, "expert", "section"),
        check_vma=False,
    )
```

```python
import jax
import jax.numpy as jnp
from jax import lax
from jax.sharding import PartitionSpec as P


def from_behind(value, axis, steps):
    count = lax.axis_size(axis)
    initial, last = (max(0, -steps), min(count, count - steps))
    return lax.ppermute(value, axis, [(source, source + steps) for source in range(initial, last)])


def ring_gather(chunk, axis, size, stride):
    index = lax.axis_index(axis)
    count = lax.axis_size(axis)
    place = (index // stride) % size

    def shifted(step):
        pairs = []
        for member in range(count):
            at = (member // stride) % size
            to = member + (((at + step) % size) - at) * stride
            pairs.append((member, to))
        return pairs

    out = jnp.zeros((size,) + chunk.shape, chunk.dtype)
    out = lax.dynamic_update_index_in_dim(out, chunk, place, 0)
    ahead, behind = chunk, chunk
    split = 0 if chunk.shape[0] % 2 == 0 else 1
    half = chunk.shape[split] // 2
    for step in range(1, size // 2 + 1):
        if step < size - step:
            ahead = lax.ppermute(ahead, axis, shifted(1))
            out = lax.dynamic_update_index_in_dim(out, ahead, (place - step) % size, 0)
            behind = lax.ppermute(behind, axis, shifted(-1))
            out = lax.dynamic_update_index_in_dim(out, behind, (place + step) % size, 0)
        else:
            front = lax.slice_in_dim(ahead, 0, half, axis=split)
            back = lax.slice_in_dim(behind, half, chunk.shape[split], axis=split)
            front = lax.ppermute(front, axis, shifted(1))
            back = lax.ppermute(back, axis, shifted(-1))
            whole = jnp.concatenate([front, back], axis=split)
            out = lax.dynamic_update_index_in_dim(out, whole, (place - step) % size, 0)
    return out


def normalize(rows):
    wide = rows.astype(jnp.float32)
    scale = lax.rsqrt(jnp.mean(wide * wide, axis=-1, keepdims=True) + 1e-05)
    return wide * scale


def processor(stream, w_first, w_second):
    normed = normalize(stream).astype(jnp.bfloat16)
    hidden = jax.nn.silu(jnp.dot(normed, w_first, preferred_element_type=jnp.float32)).astype(
        jnp.bfloat16
    )
    branch = jnp.dot(hidden, w_second, preferred_element_type=jnp.float32)
    return (stream.astype(jnp.float32) + branch).astype(jnp.bfloat16)


def local(tokens, w_in, w_out, router, exp_in, exp_out, active_rows, active_expert):
    n_section = lax.axis_size("section")
    n_expert = lax.axis_size("expert")
    section = lax.axis_index("section")
    expert_index = lax.axis_index("expert")
    micro, tok_dev, width = tokens.shape
    inner = 4 if n_expert % 4 == 0 else 1
    w_first = ring_gather(w_in[0], "expert", n_expert // inner, inner)
    w_first = ring_gather(w_first, "expert", inner, 1)
    w_first = w_first.transpose(1, 0, 2, 3).reshape(-1, width)
    w_second = ring_gather(w_out[0], "expert", inner, 1)
    w_second = ring_gather(w_second, "expert", n_expert // inner, inner)
    w_second = w_second.reshape(-1, width)
    last = n_section - 1

    def run_layer(stream):
        return processor(stream, w_first, w_second)

    def skip_layer(stream):
        return jnp.zeros_like(stream)

    groups = 3 if micro * tok_dev % 3 == 0 else micro
    chunks = tokens.reshape(groups, micro * tok_dev // groups, width)

    def tick(step, carry):
        incoming, collected = carry
        micro_index = step - section
        valid = (micro_index >= 0) & (micro_index < groups)
        clamped = jnp.clip(micro_index, 0, groups - 1)
        fresh = lax.dynamic_index_in_dim(chunks, clamped, 0, keepdims=False)
        stream = jnp.where(section == 0, fresh, incoming)
        result = lax.cond(valid, run_layer, skip_layer, stream)
        held = lax.dynamic_index_in_dim(collected, clamped, 0, keepdims=False)
        kept = jnp.where(valid & (section == last), result, held)
        collected = lax.dynamic_update_index_in_dim(collected, kept, clamped, 0)
        passed = from_behind(result, "section", 1)
        return (passed, collected)

    start = (jnp.zeros(chunks.shape[1:], jnp.bfloat16), jnp.zeros_like(chunks))
    passed, collected = lax.fori_loop(0, groups + n_section - 1, tick, start)
    rows_dev = micro * tok_dev
    flat = collected.reshape(rows_dev, width)
    n_exp = router.shape[1]
    part_width = width // n_section
    per_sub = 2
    ranks = n_section * per_sub
    chosen = active_expert[:, 0]
    onehot = chosen[:, None] == jnp.arange(n_exp, dtype=jnp.int32)[None, :]
    counts = onehot.astype(jnp.int32)
    earlier = jnp.cumsum(counts, axis=0) - counts
    rank = jnp.sum(earlier * counts, axis=1)
    picked = jnp.take(flat, active_rows, axis=0)
    contact = normalize(picked).astype(jnp.bfloat16)
    share = rank // per_sub
    slot = (share * n_exp + chosen) * per_sub + rank % per_sub
    placing = (
        jnp.arange(n_section * n_exp * per_sub, dtype=jnp.int32)[:, None] == slot[None, :]
    ).astype(jnp.bfloat16)
    dispatch = jnp.dot(placing, contact, preferred_element_type=jnp.float32).astype(jnp.bfloat16)
    dispatch = dispatch.reshape(n_section, n_exp * per_sub, width)
    columns = flat.reshape(rows_dev, n_section, part_width).transpose(1, 0, 2)
    columns = columns.reshape(n_section, rows_dev * part_width // width, width)
    def from_last(parts):
        mine = parts[last]
        for target in range(n_section - 1):
            got = lax.ppermute(parts[target], "section", [(last, target)])
            mine = jnp.where(section == target, got, mine)
        return mine

    outgoing = from_last(dispatch).reshape(n_exp, per_sub, width)
    arrived = lax.all_to_all(outgoing, "expert", split_axis=0, concat_axis=0, tiled=True)
    columns, arrived = lax.optimization_barrier((columns, arrived))
    base = from_last(columns).reshape(rows_dev, part_width)
    rows = lax.all_gather(arrived, "section", axis=0, tiled=True).reshape(-1, width)
    e_first = exp_in[0]
    e_second = exp_out[0]
    column = lax.dynamic_slice_in_dim(router, expert_index, 1, 1)
    logits = jnp.dot(rows, column, preferred_element_type=jnp.float32)[:, 0]
    gate = jax.nn.sigmoid(logits)
    hidden = jax.nn.silu(jnp.dot(rows, e_first, preferred_element_type=jnp.float32)).astype(
        jnp.bfloat16
    )
    partial_value = jnp.dot(hidden, e_second, preferred_element_type=jnp.float32)
    scaled = (gate[:, None] * partial_value).astype(jnp.bfloat16)
    summed = lax.psum_scatter(scaled, "section", scatter_dimension=1, tiled=True)
    summed = summed.reshape(n_section, n_expert, per_sub, part_width).transpose(1, 0, 2, 3)
    returned = lax.all_to_all(summed, "expert", split_axis=0, concat_axis=0, tiled=True)
    returned = returned.reshape(n_exp * ranks, part_width)
    position = chosen * ranks + rank
    added = jnp.take(returned, position, axis=0).astype(jnp.float32)
    mixed = base.astype(jnp.float32).at[active_rows].add(added)
    return mixed.astype(jnp.bfloat16).reshape(micro, tok_dev, part_width)


def solution(mesh):
    return jax.shard_map(
        local,
        mesh=mesh,
        in_specs=(
            P(None, "expert", None),
            P("section", "expert", None),
            P("section", "expert", None),
            P(),
            P("expert", None, "section"),
            P("expert", "section", None),
            P("expert"),
            P("expert", None),
        ),
        out_specs=P(None, "expert", "section"),
        check_vma=False,
    )
```

```python
import jax
import jax.numpy as jnp
from jax import lax
from jax.sharding import PartitionSpec as P


def from_behind(value, axis, steps):
    count = lax.axis_size(axis)
    initial, last = (max(0, -steps), min(count, count - steps))
    return lax.ppermute(value, axis, [(source, source + steps) for source in range(initial, last)])


def ring_gather(chunk, axis, size, stride):
    index = lax.axis_index(axis)
    count = lax.axis_size(axis)
    place = (index // stride) % size

    def shifted(step):
        pairs = []
        for member in range(count):
            at = (member // stride) % size
            to = member + (((at + step) % size) - at) * stride
            pairs.append((member, to))
        return pairs

    out = jnp.zeros((size,) + chunk.shape, chunk.dtype)
    out = lax.dynamic_update_index_in_dim(out, chunk, place, 0)
    ahead, behind = chunk, chunk
    split = 0 if chunk.shape[0] % 2 == 0 else 1
    half = chunk.shape[split] // 2
    for step in range(1, size // 2 + 1):
        if step < size - step:
            ahead = lax.ppermute(ahead, axis, shifted(1))
            out = lax.dynamic_update_index_in_dim(out, ahead, (place - step) % size, 0)
            behind = lax.ppermute(behind, axis, shifted(-1))
            out = lax.dynamic_update_index_in_dim(out, behind, (place + step) % size, 0)
        else:
            front = lax.slice_in_dim(ahead, 0, half, axis=split)
            back = lax.slice_in_dim(behind, half, chunk.shape[split], axis=split)
            front = lax.ppermute(front, axis, shifted(1))
            back = lax.ppermute(back, axis, shifted(-1))
            whole = jnp.concatenate([front, back], axis=split)
            out = lax.dynamic_update_index_in_dim(out, whole, (place - step) % size, 0)
    return out


def normalize(rows):
    wide = rows.astype(jnp.float32)
    scale = lax.rsqrt(jnp.mean(wide * wide, axis=-1, keepdims=True) + 1e-05)
    return wide * scale


def processor(stream, w_first, w_second):
    normed = normalize(stream).astype(jnp.bfloat16)
    hidden = jax.nn.silu(jnp.dot(normed, w_first, preferred_element_type=jnp.float32)).astype(
        jnp.bfloat16
    )
    branch = jnp.dot(hidden, w_second, preferred_element_type=jnp.float32)
    return (stream.astype(jnp.float32) + branch).astype(jnp.bfloat16)


def local(tokens, w_in, w_out, router, exp_in, exp_out, active_rows, active_expert):
    n_section = lax.axis_size("section")
    n_expert = lax.axis_size("expert")
    section = lax.axis_index("section")
    expert_index = lax.axis_index("expert")
    micro, tok_dev, width = tokens.shape
    inner = 4 if n_expert % 4 == 0 else 1
    w_first = ring_gather(w_in[0], "expert", n_expert // inner, inner)
    w_first = ring_gather(w_first, "expert", inner, 1)
    w_first = w_first.transpose(1, 0, 2, 3).reshape(-1, width)
    w_second = ring_gather(w_out[0], "expert", inner, 1)
    w_second = ring_gather(w_second, "expert", n_expert // inner, inner)
    w_second = w_second.reshape(-1, width)
    last = n_section - 1

    def run_layer(stream):
        return processor(stream, w_first, w_second)

    def skip_layer(stream):
        return jnp.zeros_like(stream)

    groups = 3 if micro * tok_dev % 3 == 0 else micro
    chunks = tokens.reshape(groups, micro * tok_dev // groups, width)

    def tick(step, carry):
        incoming, collected = carry
        micro_index = step - section
        valid = (micro_index >= 0) & (micro_index < groups)
        clamped = jnp.clip(micro_index, 0, groups - 1)
        fresh = lax.dynamic_index_in_dim(chunks, clamped, 0, keepdims=False)
        stream = jnp.where(section == 0, fresh, incoming)
        result = lax.cond(valid, run_layer, skip_layer, stream)
        held = lax.dynamic_index_in_dim(collected, clamped, 0, keepdims=False)
        kept = jnp.where(valid & (section == last), result, held)
        collected = lax.dynamic_update_index_in_dim(collected, kept, clamped, 0)
        passed = from_behind(result, "section", 1)
        return (passed, collected)

    start = (jnp.zeros(chunks.shape[1:], jnp.bfloat16), jnp.zeros_like(chunks))
    passed, collected = lax.fori_loop(0, groups + n_section - 1, tick, start)
    rows_dev = micro * tok_dev
    flat = collected.reshape(rows_dev, width)
    n_exp = router.shape[1]
    part_width = width // n_section
    per_sub = 2
    ranks = n_section * per_sub
    chosen = active_expert[:, 0]
    onehot = chosen[:, None] == jnp.arange(n_exp, dtype=jnp.int32)[None, :]
    counts = onehot.astype(jnp.int32)
    earlier = jnp.cumsum(counts, axis=0) - counts
    rank = jnp.sum(earlier * counts, axis=1)
    picked = jnp.take(flat, active_rows, axis=0)
    contact = normalize(picked).astype(jnp.bfloat16)
    share = rank // per_sub
    slot = (share * n_exp + chosen) * per_sub + rank % per_sub
    placing = (
        jnp.arange(n_section * n_exp * per_sub, dtype=jnp.int32)[:, None] == slot[None, :]
    ).astype(jnp.bfloat16)
    dispatch = jnp.dot(placing, contact, preferred_element_type=jnp.float32).astype(jnp.bfloat16)
    dispatch = dispatch.reshape(n_section, n_exp * per_sub, width)
    columns = flat.reshape(rows_dev, n_section, part_width).transpose(1, 0, 2)
    columns = columns.reshape(n_section, rows_dev * part_width // width, width)
    def from_last(parts):
        mine = parts[last]
        for target in range(n_section - 1):
            got = lax.ppermute(parts[target], "section", [(last, target)])
            mine = jnp.where(section == target, got, mine)
        return mine

    outgoing = from_last(dispatch).reshape(n_exp, per_sub, width)
    arrived = lax.all_to_all(outgoing, "expert", split_axis=0, concat_axis=0, tiled=True)
    columns, arrived = lax.optimization_barrier((columns, arrived))
    base = from_last(columns).reshape(rows_dev, part_width)
    rows = ring_gather(arrived.reshape(-1, width), "section", n_section, 1).reshape(-1, width)
    e_first = exp_in[0]
    e_second = exp_out[0]
    column = lax.dynamic_slice_in_dim(router, expert_index, 1, 1)
    logits = jnp.dot(rows, column, preferred_element_type=jnp.float32)[:, 0]
    gate = jax.nn.sigmoid(logits)
    hidden = jax.nn.silu(jnp.dot(rows, e_first, preferred_element_type=jnp.float32)).astype(
        jnp.bfloat16
    )
    partial_value = jnp.dot(hidden, e_second, preferred_element_type=jnp.bfloat16)
    summed = lax.psum_scatter(partial_value, "section", scatter_dimension=1, tiled=True)
    summed = (gate[:, None] * summed.astype(jnp.float32)).astype(jnp.bfloat16)
    summed = summed.reshape(n_section, n_expert, per_sub, part_width).transpose(1, 0, 2, 3)
    returned = lax.all_to_all(summed, "expert", split_axis=0, concat_axis=0, tiled=True)
    returned = returned.reshape(n_exp * ranks, part_width)
    position = chosen * ranks + rank
    added = jnp.take(returned, position, axis=0).astype(jnp.float32)
    mixed = base.astype(jnp.float32).at[active_rows].add(added)
    return mixed.astype(jnp.bfloat16).reshape(micro, tok_dev, part_width)


def solution(mesh):
    return jax.shard_map(
        local,
        mesh=mesh,
        in_specs=(
            P(None, "expert", None),
            P("section", "expert", None),
            P("section", "expert", None),
            P(),
            P("expert", None, "section"),
            P("expert", "section", None),
            P("expert"),
            P("expert", None),
        ),
        out_specs=P(None, "expert", "section"),
        check_vma=False,
    )
```

```python
import jax
import jax.numpy as jnp
from jax import lax
from jax.sharding import PartitionSpec as P


def from_behind(value, axis, steps):
    count = lax.axis_size(axis)
    initial, last = (max(0, -steps), min(count, count - steps))
    return lax.ppermute(value, axis, [(source, source + steps) for source in range(initial, last)])


def ring_gather(chunk, axis, size, stride):
    index = lax.axis_index(axis)
    count = lax.axis_size(axis)
    place = (index // stride) % size

    def shifted(step):
        pairs = []
        for member in range(count):
            at = (member // stride) % size
            to = member + (((at + step) % size) - at) * stride
            pairs.append((member, to))
        return pairs

    out = jnp.zeros((size,) + chunk.shape, chunk.dtype)
    out = lax.dynamic_update_index_in_dim(out, chunk, place, 0)
    ahead, behind = chunk, chunk
    split = 0 if chunk.shape[0] % 2 == 0 else 1
    half = chunk.shape[split] // 2
    for step in range(1, size // 2 + 1):
        if step < size - step:
            ahead = lax.ppermute(ahead, axis, shifted(1))
            out = lax.dynamic_update_index_in_dim(out, ahead, (place - step) % size, 0)
            behind = lax.ppermute(behind, axis, shifted(-1))
            out = lax.dynamic_update_index_in_dim(out, behind, (place + step) % size, 0)
        else:
            front = lax.slice_in_dim(ahead, 0, half, axis=split)
            back = lax.slice_in_dim(behind, half, chunk.shape[split], axis=split)
            front = lax.ppermute(front, axis, shifted(1))
            back = lax.ppermute(back, axis, shifted(-1))
            whole = jnp.concatenate([front, back], axis=split)
            out = lax.dynamic_update_index_in_dim(out, whole, (place - step) % size, 0)
    return out


def normalize(rows):
    wide = rows.astype(jnp.float32)
    scale = lax.rsqrt(jnp.mean(wide * wide, axis=-1, keepdims=True) + 1e-05)
    return wide * scale


def processor(stream, w_first, w_second):
    normed = normalize(stream).astype(jnp.bfloat16)
    hidden = jax.nn.silu(jnp.dot(normed, w_first, preferred_element_type=jnp.float32)).astype(
        jnp.bfloat16
    )
    branch = jnp.dot(hidden, w_second, preferred_element_type=jnp.float32)
    return (stream.astype(jnp.float32) + branch).astype(jnp.bfloat16)


def local(tokens, w_in, w_out, router, exp_in, exp_out, active_rows, active_expert):
    n_section = lax.axis_size("section")
    n_expert = lax.axis_size("expert")
    section = lax.axis_index("section")
    expert_index = lax.axis_index("expert")
    micro, tok_dev, width = tokens.shape
    inner = 4 if n_expert % 4 == 0 else 1
    w_first = ring_gather(w_in[0], "expert", n_expert // inner, inner)
    w_first = ring_gather(w_first, "expert", inner, 1)
    w_first = w_first.transpose(1, 0, 2, 3).reshape(-1, width)
    w_second = ring_gather(w_out[0], "expert", inner, 1)
    w_second = ring_gather(w_second, "expert", n_expert // inner, inner)
    w_second = w_second.reshape(-1, width)
    last = n_section - 1

    def run_layer(stream):
        return processor(stream, w_first, w_second)

    def skip_layer(stream):
        return jnp.zeros_like(stream)

    groups = 3 if micro * tok_dev % 3 == 0 else micro
    chunks = tokens.reshape(groups, micro * tok_dev // groups, width)

    def tick(step, carry):
        incoming, collected = carry
        micro_index = step - section
        valid = (micro_index >= 0) & (micro_index < groups)
        clamped = jnp.clip(micro_index, 0, groups - 1)
        fresh = lax.dynamic_index_in_dim(chunks, clamped, 0, keepdims=False)
        stream = jnp.where(section == 0, fresh, incoming)
        result = lax.cond(valid, run_layer, skip_layer, stream)
        held = lax.dynamic_index_in_dim(collected, clamped, 0, keepdims=False)
        kept = jnp.where(valid & (section == last), result, held)
        collected = lax.dynamic_update_index_in_dim(collected, kept, clamped, 0)
        passed = from_behind(result, "section", 1)
        return (passed, collected)

    start = (jnp.zeros(chunks.shape[1:], jnp.bfloat16), jnp.zeros_like(chunks))
    passed, collected = lax.fori_loop(0, groups + n_section - 1, tick, start)
    rows_dev = micro * tok_dev
    flat = collected.reshape(rows_dev, width)
    n_exp = router.shape[1]
    part_width = width // n_section
    per_sub = 2
    ranks = n_section * per_sub
    chosen = active_expert[:, 0]
    onehot = chosen[:, None] == jnp.arange(n_exp, dtype=jnp.int32)[None, :]
    counts = onehot.astype(jnp.int32)
    earlier = jnp.cumsum(counts, axis=0) - counts
    rank = jnp.sum(earlier * counts, axis=1)
    picked = jnp.take(flat, active_rows, axis=0)
    contact = normalize(picked).astype(jnp.bfloat16)
    share = rank // per_sub
    slot = (share * n_exp + chosen) * per_sub + rank % per_sub
    placing = (
        jnp.arange(n_section * n_exp * per_sub, dtype=jnp.int32)[:, None] == slot[None, :]
    ).astype(jnp.bfloat16)
    dispatch = jnp.dot(placing, contact, preferred_element_type=jnp.float32).astype(jnp.bfloat16)
    dispatch = dispatch.reshape(n_section, n_exp * per_sub, width)
    columns = flat.reshape(rows_dev, n_section, part_width).transpose(1, 0, 2)
    columns = columns.reshape(n_section, rows_dev * part_width // width, width)
    def from_last(parts):
        mine = parts[last]
        for target in range(n_section - 1):
            got = lax.ppermute(parts[target], "section", [(last, target)])
            mine = jnp.where(section == target, got, mine)
        return mine

    outgoing = from_last(dispatch).reshape(n_exp, per_sub, width)
    arrived = lax.all_to_all(outgoing, "expert", split_axis=0, concat_axis=0, tiled=True)
    columns, arrived = lax.optimization_barrier((columns, arrived))
    base = from_last(columns).reshape(rows_dev, part_width)
    rows = lax.all_gather(arrived, "section", axis=0, tiled=True).reshape(-1, width)
    e_first = exp_in[0]
    e_second = exp_out[0]
    column = lax.dynamic_slice_in_dim(router, expert_index, 1, 1)
    logits = jnp.dot(rows, column, preferred_element_type=jnp.float32)[:, 0]
    gate = jax.nn.sigmoid(logits)
    hidden = jax.nn.silu(jnp.dot(rows, e_first, preferred_element_type=jnp.float32)).astype(
        jnp.bfloat16
    )
    partial_value = jnp.dot(hidden, e_second, preferred_element_type=jnp.bfloat16)
    summed = lax.psum_scatter(partial_value, "section", scatter_dimension=1, tiled=True)
    summed = (gate[:, None] * summed.astype(jnp.float32)).astype(jnp.bfloat16)
    summed = summed.reshape(n_section, n_expert, per_sub, part_width).transpose(1, 0, 2, 3)
    returned = lax.all_to_all(summed, "expert", split_axis=0, concat_axis=0, tiled=True)
    returned = returned.reshape(n_exp * ranks, part_width)
    position = chosen * ranks + rank
    added = jnp.take(returned, position, axis=0).astype(jnp.float32)
    mixed = base.astype(jnp.float32).at[active_rows].add(added)
    return mixed.astype(jnp.bfloat16).reshape(micro, tok_dev, part_width)


def solution(mesh):
    return jax.shard_map(
        local,
        mesh=mesh,
        in_specs=(
            P(None, "expert", None),
            P("section", "expert", None),
            P("section", "expert", None),
            P(),
            P("expert", None, "section"),
            P("expert", "section", None),
            P("expert"),
            P("expert", None),
        ),
        out_specs=P(None, "expert", "section"),
        check_vma=False,
    )
```

```python
import jax
import jax.numpy as jnp
from jax import lax
from jax.sharding import PartitionSpec as P


def from_behind(value, axis, steps):
    count = lax.axis_size(axis)
    initial, last = (max(0, -steps), min(count, count - steps))
    return lax.ppermute(value, axis, [(source, source + steps) for source in range(initial, last)])


def ring_gather(chunk, axis, size, stride):
    index = lax.axis_index(axis)
    count = lax.axis_size(axis)
    place = (index // stride) % size

    def shifted(step):
        pairs = []
        for member in range(count):
            at = (member // stride) % size
            to = member + (((at + step) % size) - at) * stride
            pairs.append((member, to))
        return pairs

    out = jnp.zeros((size,) + chunk.shape, chunk.dtype)
    out = lax.dynamic_update_index_in_dim(out, chunk, place, 0)
    ahead, behind = chunk, chunk
    split = 0 if chunk.shape[0] % 2 == 0 else 1
    half = chunk.shape[split] // 2
    for step in range(1, size // 2 + 1):
        if step < size - step:
            ahead = lax.ppermute(ahead, axis, shifted(1))
            out = lax.dynamic_update_index_in_dim(out, ahead, (place - step) % size, 0)
            behind = lax.ppermute(behind, axis, shifted(-1))
            out = lax.dynamic_update_index_in_dim(out, behind, (place + step) % size, 0)
        else:
            front = lax.slice_in_dim(ahead, 0, half, axis=split)
            back = lax.slice_in_dim(behind, half, chunk.shape[split], axis=split)
            front = lax.ppermute(front, axis, shifted(1))
            back = lax.ppermute(back, axis, shifted(-1))
            whole = jnp.concatenate([front, back], axis=split)
            out = lax.dynamic_update_index_in_dim(out, whole, (place - step) % size, 0)
    return out


def normalize(rows):
    wide = rows.astype(jnp.float32)
    scale = lax.rsqrt(jnp.mean(wide * wide, axis=-1, keepdims=True) + 1e-05)
    return wide * scale


def processor(stream, w_first, w_second):
    normed = normalize(stream).astype(jnp.bfloat16)
    hidden = jax.nn.silu(jnp.dot(normed, w_first, preferred_element_type=jnp.float32)).astype(
        jnp.bfloat16
    )
    branch = jnp.dot(hidden, w_second, preferred_element_type=jnp.float32)
    return (stream.astype(jnp.float32) + branch).astype(jnp.bfloat16)


def local(tokens, w_in, w_out, router, exp_in, exp_out, active_rows, active_expert):
    n_section = lax.axis_size("section")
    n_expert = lax.axis_size("expert")
    section = lax.axis_index("section")
    expert_index = lax.axis_index("expert")
    micro, tok_dev, width = tokens.shape
    inner = 4 if n_expert % 4 == 0 else 1
    w_first = ring_gather(w_in[0], "expert", n_expert // inner, inner)
    w_first = ring_gather(w_first, "expert", inner, 1)
    w_first = w_first.transpose(1, 0, 2, 3).reshape(-1, width)
    w_second = ring_gather(w_out[0], "expert", inner, 1)
    w_second = ring_gather(w_second, "expert", n_expert // inner, inner)
    w_second = w_second.reshape(-1, width)
    last = n_section - 1

    groups = 3 if micro * tok_dev % 3 == 0 else micro
    chunks = tokens.reshape(groups, micro * tok_dev // groups, width)
    pieces = 2
    piece = width // pieces
    w_pieces = [w_second[:, j * piece:(j + 1) * piece] for j in range(pieces)]

    def tick(step, carry):
        incoming, collected = carry
        micro_index = step - section
        valid = (micro_index >= 0) & (micro_index < groups)
        clamped = jnp.clip(micro_index, 0, groups - 1)
        fresh = lax.dynamic_index_in_dim(chunks, clamped, 0, keepdims=False)
        stream = jnp.where(section == 0, fresh, incoming)
        normed = normalize(stream).astype(jnp.bfloat16)
        hidden = jax.nn.silu(
            jnp.dot(normed, w_first, preferred_element_type=jnp.float32)
        ).astype(jnp.bfloat16)
        results, passed = [], []
        for j in range(pieces):
            branch = jnp.dot(hidden, w_pieces[j], preferred_element_type=jnp.float32)
            lane = stream[:, j * piece:(j + 1) * piece].astype(jnp.float32)
            result = (lane + branch).astype(jnp.bfloat16)
            results.append(result)
            passed.append(from_behind(result, "section", 1))
        result = jnp.concatenate(results, axis=1)
        held = lax.dynamic_index_in_dim(collected, clamped, 0, keepdims=False)
        kept = jnp.where(valid & (section == last), result, held)
        collected = lax.dynamic_update_index_in_dim(collected, kept, clamped, 0)
        return (jnp.concatenate(passed, axis=1), collected)

    start = (jnp.zeros(chunks.shape[1:], jnp.bfloat16), jnp.zeros_like(chunks))
    passed, collected = lax.fori_loop(0, groups + n_section - 1, tick, start)
    rows_dev = micro * tok_dev
    flat = collected.reshape(rows_dev, width)
    n_exp = router.shape[1]
    part_width = width // n_section
    per_sub = 2
    ranks = n_section * per_sub
    chosen = active_expert[:, 0]
    onehot = chosen[:, None] == jnp.arange(n_exp, dtype=jnp.int32)[None, :]
    counts = onehot.astype(jnp.int32)
    earlier = jnp.cumsum(counts, axis=0) - counts
    rank = jnp.sum(earlier * counts, axis=1)
    picked = jnp.take(flat, active_rows, axis=0)
    contact = normalize(picked).astype(jnp.bfloat16)
    share = rank // per_sub
    slot = (share * n_exp + chosen) * per_sub + rank % per_sub
    placing = (
        jnp.arange(n_section * n_exp * per_sub, dtype=jnp.int32)[:, None] == slot[None, :]
    ).astype(jnp.bfloat16)
    dispatch = jnp.dot(placing, contact, preferred_element_type=jnp.float32).astype(jnp.bfloat16)
    dispatch = dispatch.reshape(n_section, n_exp * per_sub, width)
    columns = flat.reshape(rows_dev, n_section, part_width).transpose(1, 0, 2)
    columns = columns.reshape(n_section, rows_dev * part_width // width, width)
    def from_last(parts):
        mine = parts[last]
        for target in range(n_section - 1):
            got = lax.ppermute(parts[target], "section", [(last, target)])
            mine = jnp.where(section == target, got, mine)
        return mine

    outgoing = from_last(dispatch).reshape(n_exp, per_sub, width)
    arrived = lax.all_to_all(outgoing, "expert", split_axis=0, concat_axis=0, tiled=True)
    columns, arrived = lax.optimization_barrier((columns, arrived))
    base = from_last(columns).reshape(rows_dev, part_width)
    rows = lax.all_gather(arrived, "section", axis=0, tiled=True).reshape(-1, width)
    e_first = exp_in[0]
    e_second = exp_out[0]
    column = lax.dynamic_slice_in_dim(router, expert_index, 1, 1)
    logits = jnp.dot(rows, column, preferred_element_type=jnp.float32)[:, 0]
    gate = jax.nn.sigmoid(logits)
    hidden = jax.nn.silu(jnp.dot(rows, e_first, preferred_element_type=jnp.float32)).astype(
        jnp.bfloat16
    )
    partial_value = jnp.dot(hidden, e_second, preferred_element_type=jnp.bfloat16)
    summed = lax.psum_scatter(partial_value, "section", scatter_dimension=1, tiled=True)
    summed = (gate[:, None] * summed.astype(jnp.float32)).astype(jnp.bfloat16)
    summed = summed.reshape(n_section, n_expert, per_sub, part_width).transpose(1, 0, 2, 3)
    returned = lax.all_to_all(summed, "expert", split_axis=0, concat_axis=0, tiled=True)
    returned = returned.reshape(n_exp * ranks, part_width)
    position = chosen * ranks + rank
    added = jnp.take(returned, position, axis=0).astype(jnp.float32)
    mixed = base.astype(jnp.float32).at[active_rows].add(added)
    return mixed.astype(jnp.bfloat16).reshape(micro, tok_dev, part_width)


def solution(mesh):
    return jax.shard_map(
        local,
        mesh=mesh,
        in_specs=(
            P(None, "expert", None),
            P("section", "expert", None),
            P("section", "expert", None),
            P(),
            P("expert", None, "section"),
            P("expert", "section", None),
            P("expert"),
            P("expert", None),
        ),
        out_specs=P(None, "expert", "section"),
        check_vma=False,
    )
```

```python
import jax
import jax.numpy as jnp
from jax import lax
from jax.sharding import PartitionSpec as P


def from_behind(value, axis, steps):
    count = lax.axis_size(axis)
    initial, last = (max(0, -steps), min(count, count - steps))
    return lax.ppermute(value, axis, [(source, source + steps) for source in range(initial, last)])


def ring_gather(chunk, axis, size, stride):
    index = lax.axis_index(axis)
    count = lax.axis_size(axis)
    place = (index // stride) % size

    def shifted(step):
        pairs = []
        for member in range(count):
            at = (member // stride) % size
            to = member + (((at + step) % size) - at) * stride
            pairs.append((member, to))
        return pairs

    out = jnp.zeros((size,) + chunk.shape, chunk.dtype)
    out = lax.dynamic_update_index_in_dim(out, chunk, place, 0)
    ahead, behind = chunk, chunk
    split = 0 if chunk.shape[0] % 2 == 0 else 1
    half = chunk.shape[split] // 2
    for step in range(1, size // 2 + 1):
        if step < size - step:
            ahead = lax.ppermute(ahead, axis, shifted(1))
            out = lax.dynamic_update_index_in_dim(out, ahead, (place - step) % size, 0)
            behind = lax.ppermute(behind, axis, shifted(-1))
            out = lax.dynamic_update_index_in_dim(out, behind, (place + step) % size, 0)
        else:
            front = lax.slice_in_dim(ahead, 0, half, axis=split)
            back = lax.slice_in_dim(behind, half, chunk.shape[split], axis=split)
            front = lax.ppermute(front, axis, shifted(1))
            back = lax.ppermute(back, axis, shifted(-1))
            whole = jnp.concatenate([front, back], axis=split)
            out = lax.dynamic_update_index_in_dim(out, whole, (place - step) % size, 0)
    return out


def normalize(rows):
    wide = rows.astype(jnp.float32)
    scale = lax.rsqrt(jnp.mean(wide * wide, axis=-1, keepdims=True) + 1e-05)
    return wide * scale


def processor(stream, w_first, w_second):
    normed = normalize(stream).astype(jnp.bfloat16)
    hidden = jax.nn.silu(jnp.dot(normed, w_first, preferred_element_type=jnp.float32)).astype(
        jnp.bfloat16
    )
    branch = jnp.dot(hidden, w_second, preferred_element_type=jnp.float32)
    return (stream.astype(jnp.float32) + branch).astype(jnp.bfloat16)


def local(tokens, w_in, w_out, router, exp_in, exp_out, active_rows, active_expert):
    n_section = lax.axis_size("section")
    n_expert = lax.axis_size("expert")
    section = lax.axis_index("section")
    expert_index = lax.axis_index("expert")
    micro, tok_dev, width = tokens.shape
    inner = 4 if n_expert % 4 == 0 else 1
    w_first = ring_gather(w_in[0], "expert", n_expert // inner, inner)
    w_first = ring_gather(w_first, "expert", inner, 1)
    w_first = w_first.transpose(1, 0, 2, 3).reshape(-1, width)
    w_second = ring_gather(w_out[0], "expert", inner, 1)
    w_second = ring_gather(w_second, "expert", n_expert // inner, inner)
    w_second = w_second.reshape(-1, width)
    last = n_section - 1

    groups = 3 if micro * tok_dev % 3 == 0 else micro
    chunks = tokens.reshape(groups, micro * tok_dev // groups, width)
    pieces = 2
    piece = width // pieces
    w_pieces = [w_second[:, j * piece:(j + 1) * piece] for j in range(pieces)]

    def first_half(stream):
        normed = normalize(stream).astype(jnp.bfloat16)
        return jax.nn.silu(
            jnp.dot(normed, w_first, preferred_element_type=jnp.float32)
        ).astype(jnp.bfloat16)

    def skip_half(stream):
        return jnp.zeros(stream.shape[:1] + w_first.shape[1:], jnp.bfloat16)

    def tick(step, carry):
        incoming, collected = carry
        micro_index = step - section
        valid = (micro_index >= 0) & (micro_index < groups)
        clamped = jnp.clip(micro_index, 0, groups - 1)
        fresh = lax.dynamic_index_in_dim(chunks, clamped, 0, keepdims=False)
        stream = jnp.where(section == 0, fresh, incoming)
        hidden = lax.cond(valid, first_half, skip_half, stream)
        results, passed = [], []
        for j in range(pieces):
            branch = jnp.dot(hidden, w_pieces[j], preferred_element_type=jnp.float32)
            lane = stream[:, j * piece:(j + 1) * piece].astype(jnp.float32)
            result = (lane + branch).astype(jnp.bfloat16)
            results.append(result)
            passed.append(from_behind(result, "section", 1))
        result = jnp.concatenate(results, axis=1)
        held = lax.dynamic_index_in_dim(collected, clamped, 0, keepdims=False)
        kept = jnp.where(valid & (section == last), result, held)
        collected = lax.dynamic_update_index_in_dim(collected, kept, clamped, 0)
        return (jnp.concatenate(passed, axis=1), collected)

    start = (jnp.zeros(chunks.shape[1:], jnp.bfloat16), jnp.zeros_like(chunks))
    passed, collected = lax.fori_loop(0, groups + n_section - 1, tick, start)
    rows_dev = micro * tok_dev
    flat = collected.reshape(rows_dev, width)
    n_exp = router.shape[1]
    part_width = width // n_section
    per_sub = 2
    ranks = n_section * per_sub
    chosen = active_expert[:, 0]
    onehot = chosen[:, None] == jnp.arange(n_exp, dtype=jnp.int32)[None, :]
    counts = onehot.astype(jnp.int32)
    earlier = jnp.cumsum(counts, axis=0) - counts
    rank = jnp.sum(earlier * counts, axis=1)
    picked = jnp.take(flat, active_rows, axis=0)
    contact = normalize(picked).astype(jnp.bfloat16)
    share = rank // per_sub
    slot = (share * n_exp + chosen) * per_sub + rank % per_sub
    placing = (
        jnp.arange(n_section * n_exp * per_sub, dtype=jnp.int32)[:, None] == slot[None, :]
    ).astype(jnp.bfloat16)
    dispatch = jnp.dot(placing, contact, preferred_element_type=jnp.float32).astype(jnp.bfloat16)
    dispatch = dispatch.reshape(n_section, n_exp * per_sub, width)
    columns = flat.reshape(rows_dev, n_section, part_width).transpose(1, 0, 2)
    columns = columns.reshape(n_section, rows_dev * part_width // width, width)
    def from_last(parts):
        mine = parts[last]
        for target in range(n_section - 1):
            got = lax.ppermute(parts[target], "section", [(last, target)])
            mine = jnp.where(section == target, got, mine)
        return mine

    outgoing = from_last(dispatch).reshape(n_exp, per_sub, width)
    arrived = lax.all_to_all(outgoing, "expert", split_axis=0, concat_axis=0, tiled=True)
    columns, arrived = lax.optimization_barrier((columns, arrived))
    base = from_last(columns).reshape(rows_dev, part_width)
    rows = lax.all_gather(arrived, "section", axis=0, tiled=True).reshape(-1, width)
    e_first = exp_in[0]
    e_second = exp_out[0]
    column = lax.dynamic_slice_in_dim(router, expert_index, 1, 1)
    logits = jnp.dot(rows, column, preferred_element_type=jnp.float32)[:, 0]
    gate = jax.nn.sigmoid(logits)
    hidden = jax.nn.silu(jnp.dot(rows, e_first, preferred_element_type=jnp.float32)).astype(
        jnp.bfloat16
    )
    partial_value = jnp.dot(hidden, e_second, preferred_element_type=jnp.bfloat16)
    summed = lax.psum_scatter(partial_value, "section", scatter_dimension=1, tiled=True)
    summed = (gate[:, None] * summed.astype(jnp.float32)).astype(jnp.bfloat16)
    summed = summed.reshape(n_section, n_expert, per_sub, part_width).transpose(1, 0, 2, 3)
    returned = lax.all_to_all(summed, "expert", split_axis=0, concat_axis=0, tiled=True)
    returned = returned.reshape(n_exp * ranks, part_width)
    position = chosen * ranks + rank
    added = jnp.take(returned, position, axis=0).astype(jnp.float32)
    mixed = base.astype(jnp.float32).at[active_rows].add(added)
    return mixed.astype(jnp.bfloat16).reshape(micro, tok_dev, part_width)


def solution(mesh):
    return jax.shard_map(
        local,
        mesh=mesh,
        in_specs=(
            P(None, "expert", None),
            P("section", "expert", None),
            P("section", "expert", None),
            P(),
            P("expert", None, "section"),
            P("expert", "section", None),
            P("expert"),
            P("expert", None),
        ),
        out_specs=P(None, "expert", "section"),
        check_vma=False,
    )
```
